512 devices in a mesh: blk: 16 (over y_hi, z), bank: 32 (over y_lo, x, core).
Axes of the slice: x: 4, y: 8 (y_hi: 2, y_lo: 4; y = y_hi * 4 + y_lo), z: 8, core: 2. Of those that a mesh axis runs over, the one named last changes fastest.
Arguments:
- log_density: bfloat16 [2048, 32768], P(('blk', 'bank')), may hold values from -8 to 8
- assignment: int32 [2048], P(('blk', 'bank')), may hold values from 0 to 7, as said below
Outputs:
- centers: bfloat16 [8, 32768], P(None, 'bank')
- potentials: float32 [2048, 32768], P(('blk', 'bank'))
The draws below stay inside these ranges and needn't reach their ends.
Inputs may be any that keep to these rules, and one draw needn't show every extreme that they name: Every barycenter index is the assignment of at least one member.
All inputs are finite; a program needn't handle non-finite values.
Results may differ from the reference program's by a relative error of at most 0.0051.
Values may be sent and summed in bfloat16 or wider, within the bound.
No kernel may reach another device: no remote copies, remote signals or barrier semaphores. Data moves between devices by JAX's collectives and lax.ppermute only.
A program may use at most 64 MiB of HBM per device.

```python
import jax
import jax.numpy as jnp
from jax import lax

G = 32
M_DEV = 4
BARS = 8
ITERS = 2
CELLS = 32768
MEMBERS = 2048


def draw_assignment(key, part):
    key_order, key_rare, key_first, key_second, key_roll = jax.random.split(key, 5)
    order = jax.random.permutation(key_order, BARS)
    rare_count = BARS // 2
    rare_pick = jax.random.randint(key_rare, (MEMBERS,), 0, rare_count)
    first_pick = jax.random.randint(key_first, (MEMBERS,), rare_count, BARS)
    second_pick = jax.random.randint(key_second, (MEMBERS,), rare_count, BARS)
    common_pick = jnp.minimum(first_pick, second_pick)
    roll = jax.random.randint(key_roll, (MEMBERS,), 0, MEMBERS)
    ranked = jnp.where(roll < 2 * BARS, rare_pick, common_pick)
    member_index = jnp.arange(MEMBERS, dtype=jnp.int32)
    ranked = jnp.where(member_index < BARS, member_index, ranked)
    return order[ranked].astype(jnp.int32)


def block_scale(key, shape, cuts, low, largest):
    level, own = 1.0, jax.random.fold_in(key, 6)
    for axis_at, shards_of in cuts:
        steps = jnp.exp(jax.random.uniform(jax.random.fold_in(own, axis_at), (shards_of,), jnp.float32, low / len(cuts), largest / len(cuts)))
        level = level * jnp.repeat(steps, shape[axis_at] // shards_of).reshape([-1 if axis == axis_at else 1 for axis in range(len(shape))])
    return level


def noise(stream_key, dims, scale, most, cuts=(), kind=jnp.bfloat16):
    result = scale * jax.random.normal(stream_key, dims, jnp.float32)
    if cuts:
        result = result * block_scale(stream_key, dims, cuts, -0.22, 0.18)
    return jnp.clip(result, -most, most).astype(kind)


def setup_inputs(seed: int = 0) -> dict:
    splits = jax.random.split(jax.random.key(seed), 3)
    return {
        "log_density": noise(splits[0], (MEMBERS, CELLS), 2.0, 8.0, ((0, 512),)),
        "assignment": draw_assignment(jax.random.fold_in(splits[2], 71), 0),
    }


def kernel_tables():
    grid_pos = jnp.arange(G, dtype=jnp.float32)
    offset = grid_pos[:, None] - grid_pos[None, :]
    kernel_line = jnp.exp(-0.5 * offset * offset)
    kernel_pair = (kernel_line[:, None, :, None] * kernel_line[None, :, None, :]).reshape(G * G, G * G).astype(jnp.bfloat16)
    return kernel_line, kernel_pair


def log_convolve(field_log, kernel_line, kernel_pair):
    member_count = field_log.shape[0]
    raised = jnp.exp(field_log).astype(jnp.bfloat16).reshape(member_count * G, G * G)
    inner_sum = jnp.dot(raised, kernel_pair, preferred_element_type=jnp.float32).reshape(member_count, G, G * G)
    outer_sum = jnp.einsum("ij,mjc->mic", kernel_line, inner_sum, precision=lax.Precision.HIGHEST)
    return jnp.log(outer_sum).reshape(member_count, G * G * G)


def reference(log_density, assignment):
    kernel_line, kernel_pair = kernel_tables()
    labels = jnp.arange(BARS, dtype=jnp.int32)
    onehot = (assignment[:, None] == labels[None, :]).astype(jnp.float32)
    counts = jnp.sum(onehot, axis=0)
    groups = MEMBERS // M_DEV
    density_blocks = log_density.reshape(groups, M_DEV, CELLS)
    onehot_blocks = onehot.reshape(groups, M_DEV, BARS)
    potential = jnp.zeros((groups, M_DEV, CELLS), jnp.float32)
    centers = jnp.zeros((BARS, CELLS), jnp.bfloat16)
    for iteration in range(ITERS):
        def member_side(packed):
            density, scaling = packed
            source = density.astype(jnp.float32) - log_convolve(scaling, kernel_line, kernel_pair)
            return log_convolve(source, kernel_line, kernel_pair)
        smoothed = lax.map(member_side, (density_blocks, potential))
        sums = jnp.einsum("gmk,gmc->kc", onehot_blocks, smoothed, precision=lax.Precision.HIGHEST)
        centers = (sums / counts[:, None]).astype(jnp.bfloat16)
        chosen = jnp.einsum("gmk,kc->gmc", onehot_blocks, centers.astype(jnp.float32), precision=lax.Precision.HIGHEST)
        potential = chosen - smoothed
    return centers, potential.reshape(MEMBERS, CELLS)
```

```python
import jax
import jax.numpy as jnp
from jax import lax
from jax.sharding import PartitionSpec as P

G = 32
BARS = 8
ITERS = 2


def kernel_tables():
    grid_pos = jnp.arange(G, dtype=jnp.float32)
    offset = grid_pos[:, None] - grid_pos[None, :]
    kernel_line = jnp.exp(-0.5 * offset * offset)
    kernel_pair = (
        (kernel_line[:, None, :, None] * kernel_line[None, :, None, :])
        .reshape(G * G, G * G)
        .astype(jnp.bfloat16)
    )
    return (kernel_line, kernel_pair)


def log_convolve(field_log, kernel_line, kernel_pair):
    member_count = field_log.shape[0]
    raised = jnp.exp(field_log).astype(jnp.bfloat16).reshape(member_count * G, G * G)
    inner_sum = jnp.dot(raised, kernel_pair, preferred_element_type=jnp.float32).reshape(
        member_count, G, G * G
    )
    outer_sum = jnp.einsum("ij,mjc->mic", kernel_line, inner_sum, precision=lax.Precision.HIGHEST)
    return jnp.log(outer_sum).reshape(member_count, G * G * G)


def per_device(log_density, assignment):
    kernel_line, kernel_pair = kernel_tables()
    member_count = log_density.shape[0]
    cell_count = log_density.shape[1]
    bank_size = lax.axis_size("bank")
    owned = cell_count // bank_size
    labels = jnp.arange(BARS, dtype=jnp.int32)
    onehot = (assignment[:, None] == labels[None, :]).astype(jnp.float32)
    local_counts = jnp.sum(onehot, axis=0)
    selector = onehot.astype(jnp.bfloat16)
    member_weights = jnp.transpose(onehot)
    potential = jnp.zeros((member_count, cell_count), jnp.float32)
    counts = None
    center_all = None
    for iteration in range(ITERS):
        source = log_density.astype(jnp.float32) - log_convolve(potential, kernel_line, kernel_pair)
        smoothed = log_convolve(source, kernel_line, kernel_pair)
        local_sums = jnp.dot(member_weights, smoothed, precision=lax.Precision.HIGHEST)
        if counts is None:
            packed = jnp.concatenate(
                [local_sums, jnp.broadcast_to(local_counts[:, None], (BARS, 128))], axis=1
            )
            packed = lax.psum(packed, ("blk", "bank"))
            summed = packed[:, :cell_count]
            counts = packed[:, cell_count]
        else:
            summed = lax.psum(local_sums, ("blk", "bank"))
        center_all = (summed / counts[:, None]).astype(jnp.bfloat16)
        chosen = jnp.dot(selector, center_all, preferred_element_type=jnp.float32)
        potential = chosen - smoothed
    start = lax.axis_index("bank") * owned
    centers = lax.dynamic_slice_in_dim(center_all, start, owned, axis=1)
    return (centers, potential)


def solution(mesh):
    placed = (P(("blk", "bank"), None), P(("blk", "bank")))
    return jax.shard_map(
        per_device,
        mesh=mesh,
        in_specs=placed,
        out_specs=(P(None, "bank"), P(("blk", "bank"), None)),
        check_vma=False,
    )
```

```python
import jax
import jax.numpy as jnp
from jax import lax
from jax.sharding import PartitionSpec as P

G = 32
BARS = 8
ITERS = 2


def kernel_tables():
    grid_pos = jnp.arange(G, dtype=jnp.float32)
    offset = grid_pos[:, None] - grid_pos[None, :]
    kernel_line = jnp.exp(-0.5 * offset * offset)
    kernel_pair = (
        (kernel_line[:, None, :, None] * kernel_line[None, :, None, :])
        .reshape(G * G, G * G)
        .astype(jnp.bfloat16)
    )
    return (kernel_line, kernel_pair)


def log_convolve(field_log, kernel_line, kernel_pair):
    member_count = field_log.shape[0]
    raised = jnp.exp(field_log).astype(jnp.bfloat16).reshape(member_count * G, G * G)
    inner_sum = jnp.dot(raised, kernel_pair, preferred_element_type=jnp.float32).reshape(
        member_count, G, G * G
    )
    outer_sum = jnp.einsum("ij,mjc->mic", kernel_line, inner_sum, precision=lax.Precision.HIGHEST)
    return jnp.log(outer_sum).reshape(member_count, G * G * G)


def per_device(log_density, assignment):
    kernel_line, kernel_pair = kernel_tables()
    member_count = log_density.shape[0]
    cell_count = log_density.shape[1]
    bank_size = lax.axis_size("bank")
    owned = cell_count // bank_size
    labels = jnp.arange(BARS, dtype=jnp.int32)
    onehot = (assignment[:, None] == labels[None, :]).astype(jnp.float32)
    local_counts = jnp.sum(onehot, axis=0)
    selector = onehot.astype(jnp.bfloat16)
    member_weights = jnp.transpose(onehot)
    potential = jnp.zeros((member_count, cell_count), jnp.float32)
    counts = None
    center_all = None
    center_owned = None
    for iteration in range(ITERS):
        source = log_density.astype(jnp.float32) - log_convolve(potential, kernel_line, kernel_pair)
        smoothed = log_convolve(source, kernel_line, kernel_pair)
        blocks = smoothed.reshape(member_count, bank_size, owned)
        local_sums = jnp.einsum("km,mrc->rkc", member_weights, blocks, precision=lax.Precision.HIGHEST)
        if counts is None:
            local_sums = jnp.concatenate(
                [local_sums, jnp.broadcast_to(local_counts[None, :, None], (bank_size, BARS, 128))], axis=2
            )
        arrived = lax.all_to_all(local_sums, "bank", 0, 0, tiled=True)
        group_sums = jnp.sum(arrived, axis=0)
        summed = jnp.sum(lax.all_gather(group_sums, "blk", axis=0), axis=0)
        if counts is None:
            counts = summed[:, owned]
            summed = summed[:, :owned]
        center_owned = (summed / counts[:, None]).astype(jnp.bfloat16)
        center_all = lax.all_gather(center_owned, "bank", axis=1, tiled=True)
        chosen = jnp.dot(selector, center_all, preferred_element_type=jnp.float32)
        potential = chosen - smoothed
    centers = center_owned
    return (centers, potential)


def solution(mesh):
    placed = (P(("blk", "bank"), None), P(("blk", "bank")))
    return jax.shard_map(
        per_device,
        mesh=mesh,
        in_specs=placed,
        out_specs=(P(None, "bank"), P(("blk", "bank"), None)),
        check_vma=False,
    )
```

```python
import jax
import jax.numpy as jnp
from jax import lax
from jax.sharding import PartitionSpec as P

G = 32
BARS = 8
ITERS = 2


def kernel_tables():
    grid_pos = jnp.arange(G, dtype=jnp.float32)
    offset = grid_pos[:, None] - grid_pos[None, :]
    kernel_line = jnp.exp(-0.5 * offset * offset)
    kernel_pair = (
        (kernel_line[:, None, :, None] * kernel_line[None, :, None, :])
        .reshape(G * G, G * G)
        .astype(jnp.bfloat16)
    )
    return (kernel_line, kernel_pair)


def log_convolve(field_log, kernel_line, kernel_pair):
    member_count = field_log.shape[0]
    raised = jnp.exp(field_log).astype(jnp.bfloat16).reshape(member_count * G, G * G)
    inner_sum = jnp.dot(raised, kernel_pair, preferred_element_type=jnp.float32).reshape(
        member_count, G, G * G
    )
    outer_sum = jnp.einsum("ij,mjc->mic", kernel_line, inner_sum, precision=lax.Precision.HIGHEST)
    return jnp.log(outer_sum).reshape(member_count, G * G * G)


def per_device(log_density, assignment):
    kernel_line, kernel_pair = kernel_tables()
    member_count = log_density.shape[0]
    cell_count = log_density.shape[1]
    bank_size = lax.axis_size("bank")
    owned = cell_count // bank_size
    blk_size = lax.axis_size("blk")
    blk_levels = blk_size.bit_length() - 1
    labels = jnp.arange(BARS, dtype=jnp.int32)
    onehot = (assignment[:, None] == labels[None, :]).astype(jnp.float32)
    local_counts = jnp.sum(onehot, axis=0)
    selector = onehot.astype(jnp.bfloat16)
    member_weights = jnp.transpose(onehot)
    potential = jnp.zeros((member_count, cell_count), jnp.float32)
    counts = None
    center_all = None
    center_owned = None
    for iteration in range(ITERS):
        source = log_density.astype(jnp.float32) - log_convolve(potential, kernel_line, kernel_pair)
        smoothed = log_convolve(source, kernel_line, kernel_pair)
        blocks = smoothed.reshape(member_count, bank_size, owned)
        local_sums = jnp.einsum("km,mrc->rkc", member_weights, blocks, precision=lax.Precision.HIGHEST)
        if counts is None:
            local_sums = jnp.concatenate(
                [local_sums, jnp.broadcast_to(local_counts[None, :, None], (bank_size, BARS, 128))], axis=2
            )
        arrived = lax.all_to_all(local_sums, "bank", 0, 0, tiled=True)
        group_sums = jnp.sum(arrived, axis=0)
        summed = group_sums
        for level in range(blk_levels):
            partner = [(i, i ^ (1 << level)) for i in range(blk_size)]
            summed = summed + lax.ppermute(summed, "blk", partner)
        if counts is None:
            counts = summed[:, owned]
            summed = summed[:, :owned]
        center_owned = (summed / counts[:, None]).astype(jnp.bfloat16)
        spread = jnp.broadcast_to(center_owned[None], (bank_size, BARS, owned))
        center_all = lax.all_to_all(spread, "bank", 0, 0, tiled=True)
        chosen = jnp.einsum("mk,rkc->mrc", selector, center_all, preferred_element_type=jnp.float32)
        potential = chosen.reshape(member_count, cell_count) - smoothed
    centers = center_owned
    return (centers, potential)


def solution(mesh):
    placed = (P(("blk", "bank"), None), P(("blk", "bank")))
    return jax.shard_map(
        per_device,
        mesh=mesh,
        in_specs=placed,
        out_specs=(P(None, "bank"), P(("blk", "bank"), None)),
        check_vma=False,
    )
```

```python
import jax
import jax.numpy as jnp
from jax import lax
from jax.sharding import PartitionSpec as P

G = 32
BARS = 8
ITERS = 2


def kernel_tables():
    grid_pos = jnp.arange(G, dtype=jnp.float32)
    offset = grid_pos[:, None] - grid_pos[None, :]
    kernel_line = jnp.exp(-0.5 * offset * offset)
    row = lax.broadcasted_iota(jnp.int32, (G * G, G * G), 0)
    col = lax.broadcasted_iota(jnp.int32, (G * G, G * G), 1)

    def line_at(a, b):
        gap = a.astype(jnp.float32) - b.astype(jnp.float32)
        return jnp.exp(-0.5 * gap * gap)

    kernel_pair = (line_at(row // G, col // G) * line_at(row % G, col % G)).astype(jnp.bfloat16)
    return (kernel_line, kernel_pair)


def log_convolve(field_log, kernel_line, kernel_pair):
    member_count = field_log.shape[0]
    raised = jnp.exp(field_log).astype(jnp.bfloat16).reshape(member_count * G, G * G)
    inner_sum = jnp.dot(raised, kernel_pair, preferred_element_type=jnp.float32).reshape(
        member_count, G, G * G
    )
    outer_sum = jnp.einsum("ij,mjc->mic", kernel_line, inner_sum, precision=lax.Precision.HIGHEST)
    return jnp.log(outer_sum).reshape(member_count, G * G * G)


def per_device(log_density, assignment):
    kernel_line, kernel_pair = kernel_tables()
    member_count = log_density.shape[0]
    cell_count = log_density.shape[1]
    bank_size = lax.axis_size("bank")
    owned = cell_count // bank_size
    blk_size = lax.axis_size("blk")
    blk_levels = blk_size.bit_length() - 1
    labels = jnp.arange(BARS, dtype=jnp.int32)
    onehot = (assignment[:, None] == labels[None, :]).astype(jnp.float32)
    local_counts = jnp.sum(onehot, axis=0)
    selector = onehot.astype(jnp.bfloat16)
    member_weights = jnp.transpose(onehot)
    potential = jnp.zeros((member_count, cell_count), jnp.float32)
    counts = None
    center_all = None
    center_owned = None
    for iteration in range(ITERS):
        source = log_density.astype(jnp.float32) - log_convolve(potential, kernel_line, kernel_pair)
        smoothed = log_convolve(source, kernel_line, kernel_pair)
        blocks = smoothed.reshape(member_count, bank_size, owned)
        local_sums = jnp.einsum("km,mrc->rkc", member_weights, blocks, precision=lax.Precision.HIGHEST)
        if counts is None:
            local_sums = jnp.concatenate(
                [local_sums, jnp.broadcast_to(local_counts[None, :, None], (bank_size, BARS, 128))], axis=2
            )
        arrived = lax.all_to_all(local_sums, "bank", 0, 0, tiled=True)
        group_sums = jnp.sum(arrived, axis=0)
        summed = group_sums
        for level in range(blk_levels):
            partner = [(i, i ^ (1 << level)) for i in range(blk_size)]
            summed = summed + lax.ppermute(summed, "blk", partner)
        if counts is None:
            counts = summed[:, owned]
            summed = summed[:, :owned]
        center_owned = (summed / counts[:, None]).astype(jnp.bfloat16)
        spread = jnp.broadcast_to(center_owned[None], (bank_size, BARS, owned))
        center_all = lax.all_to_all(spread, "bank", 0, 0, tiled=True)
        chosen = jnp.einsum("mk,rkc->mrc", selector, center_all, preferred_element_type=jnp.float32)
        potential = chosen.reshape(member_count, cell_count) - smoothed
    centers = center_owned
    return (centers, potential)


def solution(mesh):
    placed = (P(("blk", "bank"), None), P(("blk", "bank")))
    return jax.shard_map(
        per_device,
        mesh=mesh,
        in_specs=placed,
        out_specs=(P(None, "bank"), P(("blk", "bank"), None)),
        check_vma=False,
    )
```

```python
import jax
import jax.numpy as jnp
from jax import lax
from jax.sharding import PartitionSpec as P

G = 32
BARS = 8
ITERS = 2


def kernel_tables():
    grid_pos = jnp.arange(G, dtype=jnp.float32)
    offset = grid_pos[:, None] - grid_pos[None, :]
    kernel_line = jnp.exp(-0.5 * offset * offset)
    row = lax.broadcasted_iota(jnp.int32, (G * G, G * G), 0)
    col = lax.broadcasted_iota(jnp.int32, (G * G, G * G), 1)

    def line_at(a, b):
        gap = a.astype(jnp.float32) - b.astype(jnp.float32)
        return jnp.exp(-0.5 * gap * gap)

    kernel_pair = (line_at(row // G, col // G) * line_at(row % G, col % G)).astype(jnp.bfloat16)
    return (kernel_line, lax.optimization_barrier(kernel_pair))


def log_convolve(field_log, kernel_line, kernel_pair):
    member_count = field_log.shape[0]
    raised = jnp.exp(field_log).astype(jnp.bfloat16).reshape(member_count * G, G * G)
    inner_sum = jnp.dot(raised, kernel_pair, preferred_element_type=jnp.float32).reshape(
        member_count, G, G * G
    )
    outer_sum = jnp.einsum("ij,mjc->mic", kernel_line, inner_sum, precision=lax.Precision.HIGHEST)
    return jnp.log(outer_sum).reshape(member_count, G * G * G)


def per_device(log_density, assignment):
    kernel_line, kernel_pair = kernel_tables()
    member_count = log_density.shape[0]
    cell_count = log_density.shape[1]
    bank_size = lax.axis_size("bank")
    owned = cell_count // bank_size
    blk_size = lax.axis_size("blk")
    blk_levels = blk_size.bit_length() - 1
    labels = jnp.arange(BARS, dtype=jnp.int32)
    onehot = (assignment[:, None] == labels[None, :]).astype(jnp.float32)
    local_counts = jnp.sum(onehot, axis=0)
    selector = onehot.astype(jnp.bfloat16)
    member_weights = jnp.transpose(onehot)
    potential = jnp.zeros((member_count, cell_count), jnp.float32)
    counts = None
    center_all = None
    center_owned = None
    for iteration in range(ITERS):
        source = log_density.astype(jnp.float32) - log_convolve(potential, kernel_line, kernel_pair)
        smoothed = log_convolve(source, kernel_line, kernel_pair)
        blocks = smoothed.reshape(member_count, bank_size, owned)
        local_sums = jnp.einsum("km,mrc->rkc", member_weights, blocks, precision=lax.Precision.HIGHEST)
        if counts is None:
            local_sums = jnp.concatenate(
                [local_sums, jnp.broadcast_to(local_counts[None, :, None], (bank_size, BARS, 128))], axis=2
            )
        arrived = lax.all_to_all(local_sums, "bank", 0, 0, tiled=True)
        group_sums = jnp.sum(arrived, axis=0)
        summed = group_sums
        level = 0
        while level < blk_levels:
            if level + 1 < blk_levels:
                near, far = 1 << level, 2 << level
                got = [
                    lax.ppermute(summed, "blk", [(i, i ^ step) for i in range(blk_size)])
                    for step in (near, far, near | far)
                ]
                summed = (summed + got[0]) + (got[1] + got[2])
                level += 2
            else:
                partner = [(i, i ^ (1 << level)) for i in range(blk_size)]
                summed = summed + lax.ppermute(summed, "blk", partner)
                level += 1
        if counts is None:
            counts = summed[:, owned]
            summed = summed[:, :owned]
        center_owned = (summed / counts[:, None]).astype(jnp.bfloat16)
        spread = jnp.broadcast_to(center_owned[None], (bank_size, BARS, owned))
        center_all = lax.all_to_all(spread, "bank", 0, 0, tiled=True)
        chosen = jnp.einsum("mk,rkc->mrc", selector, center_all, preferred_element_type=jnp.float32)
        potential = chosen.reshape(member_count, cell_count) - smoothed
    centers = center_owned
    return (centers, potential)


def solution(mesh):
    placed = (P(("blk", "bank"), None), P(("blk", "bank")))
    return jax.shard_map(
        per_device,
        mesh=mesh,
        in_specs=placed,
        out_specs=(P(None, "bank"), P(("blk", "bank"), None)),
        check_vma=False,
    )
```

```python
import jax
import jax.numpy as jnp
from jax import lax
from jax.sharding import PartitionSpec as P

G = 32
BARS = 8
ITERS = 2


def kernel_tables():
    grid_pos = jnp.arange(G, dtype=jnp.float32)
    offset = grid_pos[:, None] - grid_pos[None, :]
    kernel_line = jnp.exp(-0.5 * offset * offset)
    row = lax.broadcasted_iota(jnp.int32, (G * G, G * G), 0)
    col = lax.broadcasted_iota(jnp.int32, (G * G, G * G), 1)

    def line_at(a, b):
        gap = a.astype(jnp.float32) - b.astype(jnp.float32)
        return jnp.exp(-0.5 * gap * gap)

    kernel_pair = (line_at(row // G, col // G) * line_at(row % G, col % G)).astype(jnp.bfloat16)
    return (kernel_line, lax.optimization_barrier(kernel_pair))


def log_convolve(field_log, kernel_line, kernel_pair):
    member_count = field_log.shape[0]
    raised = jnp.exp(field_log).astype(jnp.bfloat16).reshape(member_count * G, G * G)
    inner_sum = jnp.dot(raised, kernel_pair, preferred_element_type=jnp.float32).reshape(
        member_count, G, G * G
    )
    outer_sum = jnp.einsum("ij,mjc->mic", kernel_line, inner_sum, precision=lax.Precision.HIGHEST)
    return jnp.log(outer_sum).reshape(member_count, G * G * G)


def per_device(log_density, assignment):
    kernel_line, kernel_pair = kernel_tables()
    member_count = log_density.shape[0]
    cell_count = log_density.shape[1]
    bank_size = lax.axis_size("bank")
    owned = cell_count // bank_size
    blk_size = lax.axis_size("blk")
    blk_levels = blk_size.bit_length() - 1
    labels = jnp.arange(BARS, dtype=jnp.int32)
    onehot = (assignment[:, None] == labels[None, :]).astype(jnp.float32)
    selector = onehot.astype(jnp.bfloat16)
    potential = jnp.zeros((member_count, cell_count), jnp.float32)
    counts = None
    weights_in = None
    center_owned = None
    for iteration in range(ITERS):
        source = log_density.astype(jnp.float32) - log_convolve(potential, kernel_line, kernel_pair)
        smoothed = log_convolve(source, kernel_line, kernel_pair)
        rows = jnp.transpose(smoothed.reshape(member_count, bank_size, owned), (1, 0, 2))
        if weights_in is None:
            label_lanes = jnp.broadcast_to(
                assignment.astype(jnp.float32)[None, :, None], (bank_size, member_count, 128)
            )
            rows = jnp.concatenate([rows, label_lanes], axis=2)
        arrived = lax.all_to_all(rows, "bank", 0, 0, tiled=True)
        if weights_in is None:
            weights_in = (arrived[:, :, owned, None] == labels.astype(jnp.float32)).astype(jnp.float32)
            arrived = arrived[:, :, :owned]
        group_sums = jnp.einsum("smk,smc->kc", weights_in, arrived, precision=lax.Precision.HIGHEST)
        if counts is None:
            group_counts = jnp.sum(weights_in, axis=(0, 1))
            group_sums = jnp.concatenate(
                [group_sums, jnp.broadcast_to(group_counts[:, None], (BARS, 128))], axis=1
            )
        summed = group_sums
        for level in range(blk_levels):
            partner = [(i, i ^ (1 << level)) for i in range(blk_size)]
            summed = summed + lax.ppermute(summed, "blk", partner)
        if counts is None:
            counts = summed[:, owned]
            summed = summed[:, :owned]
        center_owned = (summed / counts[:, None]).astype(jnp.bfloat16)
        spread = jnp.broadcast_to(center_owned[None], (bank_size, BARS, owned))
        center_all = lax.all_to_all(spread, "bank", 0, 0, tiled=True)
        chosen = jnp.einsum("mk,rkc->mrc", selector, center_all, preferred_element_type=jnp.float32)
        potential = chosen.reshape(member_count, cell_count) - smoothed
    centers = center_owned
    return (centers, potential)


def solution(mesh):
    placed = (P(("blk", "bank"), None), P(("blk", "bank")))
    return jax.shard_map(
        per_device,
        mesh=mesh,
        in_specs=placed,
        out_specs=(P(None, "bank"), P(("blk", "bank"), None)),
        check_vma=False,
    )
```

```python
import jax
import jax.numpy as jnp
from jax import lax
from jax.sharding import Mesh, PartitionSpec as P

G = 32
BARS = 8
ITERS = 2


def kernel_tables():
    grid_pos = jnp.arange(G, dtype=jnp.float32)
    offset = grid_pos[:, None] - grid_pos[None, :]
    kernel_line = jnp.exp(-0.5 * offset * offset)
    row = lax.broadcasted_iota(jnp.int32, (G * G, G * G), 0)
    col = lax.broadcasted_iota(jnp.int32, (G * G, G * G), 1)

    def line_at(a, b):
        gap = a.astype(jnp.float32) - b.astype(jnp.float32)
        return jnp.exp(-0.5 * gap * gap)

    kernel_pair = (line_at(row // G, col // G) * line_at(row % G, col % G)).astype(jnp.bfloat16)
    return (kernel_line, lax.optimization_barrier(kernel_pair))


def log_convolve(field_log, kernel_line, kernel_pair):
    member_count = field_log.shape[0]
    raised = jnp.exp(field_log).astype(jnp.bfloat16).reshape(member_count * G, G * G)
    inner_sum = jnp.dot(raised, kernel_pair, preferred_element_type=jnp.float32).reshape(
        member_count, G, G * G
    )
    outer_sum = jnp.einsum("ij,mjc->mic", kernel_line, inner_sum, precision=lax.Precision.HIGHEST)
    return jnp.log(outer_sum).reshape(member_count, G * G * G)


def per_device(log_density, assignment):
    kernel_line, kernel_pair = kernel_tables()
    member_count = log_density.shape[0]
    cell_count = log_density.shape[1]
    spread_axes = ("hi", "bank")
    spread_size = lax.axis_size("hi") * lax.axis_size("bank")
    z_size = lax.axis_size("z")
    chunk = cell_count // spread_size
    owned = cell_count // lax.axis_size("bank")
    labels = jnp.arange(BARS, dtype=jnp.int32)
    onehot = (assignment[:, None] == labels[None, :]).astype(jnp.float32)
    selector = onehot.astype(jnp.bfloat16)
    potential = jnp.zeros((member_count, cell_count), jnp.float32)
    counts = None
    weights_in = None
    center_all = None
    for iteration in range(ITERS):
        source = log_density.astype(jnp.float32) - log_convolve(potential, kernel_line, kernel_pair)
        smoothed = log_convolve(source, kernel_line, kernel_pair)
        rows = jnp.transpose(smoothed.reshape(member_count, spread_size, chunk), (1, 0, 2))
        if weights_in is None:
            label_lanes = jnp.broadcast_to(
                assignment.astype(jnp.float32)[None, :, None], (spread_size, member_count, 128)
            )
            rows = jnp.concatenate([rows, label_lanes], axis=2)
        arrived = lax.all_to_all(rows, spread_axes, 0, 0, tiled=True)
        if weights_in is None:
            weights_in = (arrived[:, :, chunk, None] == labels.astype(jnp.float32)).astype(jnp.float32)
            arrived = arrived[:, :, :chunk]
        group_sums = jnp.einsum("smk,smc->kc", weights_in, arrived, precision=lax.Precision.HIGHEST)
        if counts is None:
            group_counts = jnp.sum(weights_in, axis=(0, 1))
            group_sums = jnp.concatenate(
                [group_sums, jnp.broadcast_to(group_counts[:, None], (BARS, 128))], axis=1
            )
        peers = jnp.broadcast_to(group_sums[None], (z_size,) + group_sums.shape)
        summed = jnp.sum(lax.all_to_all(peers, "z", 0, 0, tiled=True), axis=0)
        if counts is None:
            counts = summed[:, chunk]
            summed = summed[:, :chunk]
        center_chunk = (summed / counts[:, None]).astype(jnp.bfloat16)
        spread = jnp.broadcast_to(center_chunk[None], (spread_size, BARS, chunk))
        center_all = lax.all_to_all(spread, spread_axes, 0, 0, tiled=True)
        chosen = jnp.einsum("mk,jkc->mjc", selector, center_all, preferred_element_type=jnp.float32)
        potential = chosen.reshape(member_count, cell_count) - smoothed
    per_owned = owned // chunk
    mine = lax.dynamic_slice_in_dim(center_all, lax.axis_index("bank") * per_owned, per_owned, axis=0)
    centers = jnp.transpose(mine, (1, 0, 2)).reshape(BARS, owned)
    return (centers, potential)


def solution(mesh):
    blk_size = mesh.shape["blk"]
    hi_size = 2 if blk_size % 2 == 0 else 1
    devices = mesh.devices.reshape(hi_size, blk_size // hi_size, mesh.shape["bank"])
    view = Mesh(devices, ("hi", "z", "bank"))
    placed = (P(("hi", "z", "bank"), None), P(("hi", "z", "bank")))
    return jax.shard_map(
        per_device,
        mesh=view,
        in_specs=placed,
        out_specs=(P(None, "bank"), P(("hi", "z", "bank"), None)),
        check_vma=False,
    )
```

```python
import jax
import jax.numpy as jnp
from jax import lax
from jax.sharding import Mesh, PartitionSpec as P

G = 32
BARS = 8
ITERS = 2


def kernel_tables():
    grid_pos = jnp.arange(G, dtype=jnp.float32)
    offset = grid_pos[:, None] - grid_pos[None, :]
    kernel_line = jnp.exp(-0.5 * offset * offset)
    row = lax.broadcasted_iota(jnp.int32, (G * G, G * G), 0)
    col = lax.broadcasted_iota(jnp.int32, (G * G, G * G), 1)

    def line_at(a, b):
        gap = a.astype(jnp.float32) - b.astype(jnp.float32)
        return jnp.exp(-0.5 * gap * gap)

    kernel_pair = (line_at(row // G, col // G) * line_at(row % G, col % G)).astype(jnp.bfloat16)
    return (kernel_line, lax.optimization_barrier(kernel_pair))


def log_convolve(field_log, kernel_line, kernel_pair):
    member_count = field_log.shape[0]
    raised = jnp.exp(field_log).astype(jnp.bfloat16).reshape(member_count * G, G * G)
    inner_sum = jnp.dot(raised, kernel_pair, preferred_element_type=jnp.float32).reshape(
        member_count, G, G * G
    )
    outer_sum = jnp.einsum("ij,mjc->mic", kernel_line, inner_sum, precision=lax.Precision.HIGHEST)
    return jnp.log(outer_sum).reshape(member_count, G * G * G)


def per_device(log_density, assignment):
    kernel_line, kernel_pair = kernel_tables()
    member_count = log_density.shape[0]
    cell_count = log_density.shape[1]
    spread_axes = ("bank", "hi")
    spread_size = lax.axis_size("hi") * lax.axis_size("bank")
    z_size = lax.axis_size("z")
    chunk = cell_count // spread_size
    labels = jnp.arange(BARS, dtype=jnp.int32)
    onehot = (assignment[:, None] == labels[None, :]).astype(jnp.float32)
    potential = jnp.zeros((member_count, cell_count), jnp.float32)
    counts = None
    weights_in = None
    center_chunk = None
    for iteration in range(ITERS):
        source = log_density.astype(jnp.float32) - log_convolve(potential, kernel_line, kernel_pair)
        smoothed = log_convolve(source, kernel_line, kernel_pair)
        rows = jnp.transpose(smoothed.reshape(member_count, spread_size, chunk), (1, 0, 2))
        if weights_in is None:
            label_lanes = jnp.broadcast_to(
                assignment.astype(jnp.float32)[None, :, None], (spread_size, member_count, 128)
            )
            rows = jnp.concatenate([rows, label_lanes], axis=2)
        arrived = lax.all_to_all(rows, spread_axes, 0, 0, tiled=True)
        if weights_in is None:
            weights_in = (arrived[:, :, chunk, None] == labels.astype(jnp.float32)).astype(jnp.float32)
            arrived = arrived[:, :, :chunk]
        group_sums = jnp.einsum("smk,smc->kc", weights_in, arrived, precision=lax.Precision.HIGHEST)
        if counts is None:
            group_counts = jnp.sum(weights_in, axis=(0, 1))
            group_sums = jnp.concatenate(
                [group_sums, jnp.broadcast_to(group_counts[:, None], (BARS, 128))], axis=1
            )
        peers = jnp.broadcast_to(group_sums[None], (z_size,) + group_sums.shape)
        summed = jnp.sum(lax.all_to_all(peers, "z", 0, 0, tiled=True), axis=0)
        if counts is None:
            counts = summed[:, chunk]
            summed = summed[:, :chunk]
        center_chunk = (summed / counts[:, None]).astype(jnp.bfloat16)
        wanted = jnp.einsum(
            "smk,kc->smc", weights_in.astype(jnp.bfloat16), center_chunk, preferred_element_type=jnp.float32
        ).astype(jnp.bfloat16)
        returned = lax.all_to_all(wanted, spread_axes, 0, 0, tiled=True)
        chosen = jnp.transpose(returned, (1, 0, 2)).reshape(member_count, cell_count)
        potential = chosen.astype(jnp.float32) - smoothed
    other = lax.ppermute(center_chunk, "hi", [(0, 1), (1, 0)])
    first = lax.axis_index("hi") == 0
    centers = jnp.concatenate(
        [jnp.where(first, center_chunk, other), jnp.where(first, other, center_chunk)], axis=1
    )
    return (centers, potential)


def solution(mesh):
    blk_size = mesh.shape["blk"]
    hi_size = 2 if blk_size % 2 == 0 else 1
    devices = mesh.devices.reshape(hi_size, blk_size // hi_size, mesh.shape["bank"])
    view = Mesh(devices, ("hi", "z", "bank"))
    placed = (P(("hi", "z", "bank"), None), P(("hi", "z", "bank")))
    return jax.shard_map(
        per_device,
        mesh=view,
        in_specs=placed,
        out_specs=(P(None, "bank"), P(("hi", "z", "bank"), None)),
        check_vma=False,
    )
```

```python
import jax
import jax.numpy as jnp
from jax import lax
from jax.sharding import Mesh, PartitionSpec as P

G = 32
BARS = 8
ITERS = 2


def kernel_tables():
    grid_pos = jnp.arange(G, dtype=jnp.float32)
    offset = grid_pos[:, None] - grid_pos[None, :]
    kernel_line = jnp.exp(-0.5 * offset * offset)
    row = lax.broadcasted_iota(jnp.int32, (G * G, G * G), 0)
    col = lax.broadcasted_iota(jnp.int32, (G * G, G * G), 1)

    def line_at(a, b):
        gap = a.astype(jnp.float32) - b.astype(jnp.float32)
        return jnp.exp(-0.5 * gap * gap)

    kernel_pair = (line_at(row // G, col // G) * line_at(row % G, col % G)).astype(jnp.bfloat16)
    return (kernel_line, lax.optimization_barrier(kernel_pair))


def log_convolve(field_log, kernel_line, kernel_pair):
    member_count = field_log.shape[0]
    raised = jnp.exp(field_log).astype(jnp.bfloat16).reshape(member_count * G, G * G)
    inner_sum = jnp.dot(raised, kernel_pair, preferred_element_type=jnp.float32).reshape(
        member_count, G, G * G
    )
    outer_sum = jnp.einsum("ij,mjc->mic", kernel_line, inner_sum, precision=lax.Precision.HIGHEST)
    return jnp.log(outer_sum).reshape(member_count, G * G * G)


def per_device(log_density, assignment):
    kernel_line, kernel_pair = kernel_tables()
    member_count = log_density.shape[0]
    cell_count = log_density.shape[1]
    spread_axes = ("bank", "hi")
    spread_size = lax.axis_size("hi") * lax.axis_size("bank")
    z_size = lax.axis_size("z")
    chunk = cell_count // spread_size
    labels = jnp.arange(BARS, dtype=jnp.int32)
    onehot = (assignment[:, None] == labels[None, :]).astype(jnp.float32)
    potential = jnp.zeros((member_count, cell_count), jnp.float32)
    counts = None
    weights_in = None
    center_chunk = None
    for iteration in range(ITERS):
        if iteration == 0:
            flat = log_convolve(jnp.zeros((1, cell_count), jnp.float32), kernel_line, kernel_pair)
            source = log_density.astype(jnp.float32) - flat
        else:
            source = log_density.astype(jnp.float32) - log_convolve(potential, kernel_line, kernel_pair)
        smoothed = log_convolve(source, kernel_line, kernel_pair)
        rows = smoothed.reshape(member_count, spread_size, chunk)
        if weights_in is None:
            label_lanes = jnp.broadcast_to(
                assignment.astype(jnp.float32)[:, None, None], (member_count, spread_size, 128)
            )
            rows = jnp.concatenate([rows, label_lanes], axis=2)
        arrived = lax.all_to_all(rows, spread_axes, 1, 1, tiled=True)
        if weights_in is None:
            weights_in = (arrived[:, :, chunk, None] == labels.astype(jnp.float32)).astype(jnp.float32)
            arrived = arrived[:, :, :chunk]
        group_sums = jnp.einsum("msk,msc->kc", weights_in, arrived, precision=lax.Precision.HIGHEST)
        if counts is None:
            group_counts = jnp.sum(weights_in, axis=(0, 1))
            group_sums = jnp.concatenate(
                [group_sums, jnp.broadcast_to(group_counts[:, None], (BARS, 128))], axis=1
            )
        peers = jnp.broadcast_to(group_sums[None], (z_size,) + group_sums.shape)
        summed = jnp.sum(lax.all_to_all(peers, "z", 0, 0, tiled=True), axis=0)
        if counts is None:
            counts = summed[:, chunk]
            summed = summed[:, :chunk]
        center_chunk = (summed / counts[:, None]).astype(jnp.bfloat16)
        wanted = jnp.einsum(
            "msk,kc->msc", weights_in.astype(jnp.bfloat16), center_chunk, preferred_element_type=jnp.float32
        ).astype(jnp.bfloat16)
        returned = lax.all_to_all(wanted, spread_axes, 1, 1, tiled=True)
        chosen = returned.reshape(member_count, cell_count)
        potential = chosen.astype(jnp.float32) - smoothed
    other = lax.ppermute(center_chunk, "hi", [(0, 1), (1, 0)])
    first = lax.axis_index("hi") == 0
    centers = jnp.concatenate(
        [jnp.where(first, center_chunk, other), jnp.where(first, other, center_chunk)], axis=1
    )
    return (centers, potential)


def solution(mesh):
    blk_size = mesh.shape["blk"]
    hi_size = 2 if blk_size % 2 == 0 else 1
    devices = mesh.devices.reshape(hi_size, blk_size // hi_size, mesh.shape["bank"])
    view = Mesh(devices, ("hi", "z", "bank"))
    placed = (P(("hi", "z", "bank"), None), P(("hi", "z", "bank")))
    return jax.shard_map(
        per_device,
        mesh=view,
        in_specs=placed,
        out_specs=(P(None, "bank"), P(("hi", "z", "bank"), None)),
        check_vma=False,
    )
```

```python
import jax
import jax.numpy as jnp
from jax import lax
from jax.sharding import Mesh, PartitionSpec as P

G = 32
BARS = 8
ITERS = 2


def kernel_tables():
    grid_pos = jnp.arange(G, dtype=jnp.float32)
    offset = grid_pos[:, None] - grid_pos[None, :]
    kernel_line = jnp.exp(-0.5 * offset * offset)
    row = lax.broadcasted_iota(jnp.int32, (G * G, G * G), 0)
    col = lax.broadcasted_iota(jnp.int32, (G * G, G * G), 1)

    def line_at(a, b):
        gap = a.astype(jnp.float32) - b.astype(jnp.float32)
        return jnp.exp(-0.5 * gap * gap)

    kernel_pair = (line_at(row // G, col // G) * line_at(row % G, col % G)).astype(jnp.bfloat16)
    return (kernel_line, lax.optimization_barrier(kernel_pair))


def log_convolve(field_log, kernel_line, kernel_pair):
    member_count = field_log.shape[0]
    raised = jnp.exp(field_log).astype(jnp.bfloat16).reshape(member_count * G, G * G)
    inner_sum = jnp.dot(raised, kernel_pair, preferred_element_type=jnp.float32).reshape(
        member_count, G, G * G
    )
    outer_sum = jnp.einsum("ij,mjc->mic", kernel_line, inner_sum, precision=lax.Precision.HIGHEST)
    return jnp.log(outer_sum).reshape(member_count, G * G * G)


def per_device(log_density, assignment):
    kernel_line, kernel_pair = kernel_tables()
    member_count = log_density.shape[0]
    cell_count = log_density.shape[1]
    spread_axes = ("bank", "hi")
    spread_size = lax.axis_size("hi") * lax.axis_size("bank")
    z_size = lax.axis_size("z")
    chunk = cell_count // spread_size
    labels = jnp.arange(BARS, dtype=jnp.int32)
    onehot = (assignment[:, None] == labels[None, :]).astype(jnp.float32)
    potential = jnp.zeros((member_count, cell_count), jnp.float32)
    counts = None
    weights_in = None
    center_chunk = None
    for iteration in range(ITERS):
        if iteration == 0:
            flat = log_convolve(jnp.zeros((1, cell_count), jnp.float32), kernel_line, kernel_pair)
            source = log_density.astype(jnp.float32) - flat
        else:
            source = log_density.astype(jnp.float32) - log_convolve(potential, kernel_line, kernel_pair)
        smoothed = log_convolve(source, kernel_line, kernel_pair)
        rows = smoothed.reshape(member_count, spread_size, chunk)
        if weights_in is None:
            label_lanes = jnp.broadcast_to(
                assignment.astype(jnp.float32)[:, None, None], (member_count, spread_size, 128)
            )
            rows = jnp.concatenate([rows, label_lanes], axis=2)
        arrived = lax.all_to_all(rows, spread_axes, 1, 1, tiled=True)
        if weights_in is None:
            label_in = jnp.max(arrived[:, :, chunk:], axis=2)
            weights_in = (label_in[:, :, None] == labels.astype(jnp.float32)).astype(jnp.float32)
            arrived = arrived[:, :, :chunk]
        group_sums = jnp.einsum("msk,msc->kc", weights_in, arrived, precision=lax.Precision.HIGHEST)
        if counts is None:
            group_counts = jnp.sum(weights_in, axis=(0, 1))
            group_sums = jnp.concatenate(
                [group_sums, jnp.broadcast_to(group_counts[:, None], (BARS, 128))], axis=1
            )
        peers = jnp.broadcast_to(group_sums[None], (z_size,) + group_sums.shape)
        summed = jnp.sum(lax.all_to_all(peers, "z", 0, 0, tiled=True), axis=0)
        if counts is None:
            counts = summed[:, chunk]
            summed = summed[:, :chunk]
        center_chunk = (summed / counts[:, None]).astype(jnp.bfloat16)
        wanted = jnp.einsum(
            "msk,kc->msc", weights_in.astype(jnp.bfloat16), center_chunk, preferred_element_type=jnp.float32
        ).astype(jnp.bfloat16)
        returned = lax.all_to_all(wanted, spread_axes, 1, 1, tiled=True)
        chosen = returned.reshape(member_count, cell_count)
        potential = chosen.astype(jnp.float32) - smoothed
    other = lax.ppermute(center_chunk, "hi", [(0, 1), (1, 0)])
    first = lax.axis_index("hi") == 0
    centers = jnp.concatenate(
        [jnp.where(first, center_chunk, other), jnp.where(first, other, center_chunk)], axis=1
    )
    return (centers, potential)


def solution(mesh):
    blk_size = mesh.shape["blk"]
    hi_size = 2 if blk_size % 2 == 0 else 1
    devices = mesh.devices.reshape(hi_size, blk_size // hi_size, mesh.shape["bank"])
    view = Mesh(devices, ("hi", "z", "bank"))
    placed = (P(("hi", "z", "bank"), None), P(("hi", "z", "bank")))
    return jax.shard_map(
        per_device,
        mesh=view,
        in_specs=placed,
        out_specs=(P(None, "bank"), P(("hi", "z", "bank"), None)),
        check_vma=False,
    )
```

```python
import jax
import ml_dtypes
import numpy as np
import jax.numpy as jnp
from jax import lax
from jax.sharding import Mesh, PartitionSpec as P

G = 32
BARS = 8
ITERS = 2


def kernel_tables():
    grid_pos = jnp.arange(G, dtype=jnp.float32)
    offset = grid_pos[:, None] - grid_pos[None, :]
    kernel_line = jnp.exp(-0.5 * offset * offset)
    line_np = np.arange(G, dtype=np.float32)
    gap = line_np[:, None] - line_np[None, :]
    line_np = np.exp(np.float32(-0.5) * gap * gap).astype(np.float32)
    pair_np = (line_np[:, None, :, None] * line_np[None, :, None, :]).reshape(G * G, G * G)
    kernel_pair = jnp.asarray(pair_np.astype(ml_dtypes.bfloat16))
    return (kernel_line, kernel_pair)


def log_convolve(field_log, kernel_line, kernel_pair):
    member_count = field_log.shape[0]
    raised = jnp.exp(field_log).astype(jnp.bfloat16).reshape(member_count * G, G * G)
    inner_sum = jnp.dot(raised, kernel_pair, preferred_element_type=jnp.float32).reshape(
        member_count, G, G * G
    )
    outer_sum = jnp.einsum("ij,mjc->mic", kernel_line, inner_sum, precision=lax.Precision.HIGHEST)
    return jnp.log(outer_sum).reshape(member_count, G * G * G)


def per_device(log_density, assignment):
    kernel_line, kernel_pair = kernel_tables()
    member_count = log_density.shape[0]
    cell_count = log_density.shape[1]
    spread_axes = ("bank", "hi")
    spread_size = lax.axis_size("hi") * lax.axis_size("bank")
    z_size = lax.axis_size("z")
    chunk = cell_count // spread_size
    labels = jnp.arange(BARS, dtype=jnp.int32)
    onehot = (assignment[:, None] == labels[None, :]).astype(jnp.float32)
    potential = jnp.zeros((member_count, cell_count), jnp.float32)
    counts = None
    weights_in = None
    center_chunk = None
    for iteration in range(ITERS):
        if iteration == 0:
            flat = log_convolve(jnp.zeros((1, cell_count), jnp.float32), kernel_line, kernel_pair)
            source = log_density.astype(jnp.float32) - flat
        else:
            source = log_density.astype(jnp.float32) - log_convolve(potential, kernel_line, kernel_pair)
        smoothed = log_convolve(source, kernel_line, kernel_pair)
        rows = smoothed.reshape(member_count, spread_size, chunk)
        if weights_in is None:
            label_lanes = jnp.broadcast_to(
                assignment.astype(jnp.float32)[:, None, None], (member_count, spread_size, 128)
            )
            rows = jnp.concatenate([rows, label_lanes], axis=2)
        arrived = lax.all_to_all(rows, spread_axes, 1, 1, tiled=True)
        if weights_in is None:
            weights_in = (arrived[:, :, chunk, None] == labels.astype(jnp.float32)).astype(jnp.float32)
            arrived = arrived[:, :, :chunk]
        group_sums = jnp.einsum("msk,msc->kc", weights_in, arrived, precision=lax.Precision.HIGHEST)
        if counts is None:
            group_counts = jnp.sum(weights_in, axis=(0, 1))
            group_sums = jnp.concatenate(
                [group_sums, jnp.broadcast_to(group_counts[:, None], (BARS, 128))], axis=1
            )
        peers = jnp.broadcast_to(group_sums[None], (z_size,) + group_sums.shape)
        summed = jnp.sum(lax.all_to_all(peers, "z", 0, 0, tiled=True), axis=0)
        if counts is None:
            counts = summed[:, chunk]
            summed = summed[:, :chunk]
        center_chunk = (summed / counts[:, None]).astype(jnp.bfloat16)
        wanted = jnp.einsum(
            "msk,kc->msc", weights_in.astype(jnp.bfloat16), center_chunk, preferred_element_type=jnp.float32
        ).astype(jnp.bfloat16)
        returned = lax.all_to_all(wanted, spread_axes, 1, 1, tiled=True)
        chosen = returned.reshape(member_count, cell_count)
        potential = chosen.astype(jnp.float32) - smoothed
    other = lax.ppermute(center_chunk, "hi", [(0, 1), (1, 0)])
    first = lax.axis_index("hi") == 0
    centers = jnp.concatenate(
        [jnp.where(first, center_chunk, other), jnp.where(first, other, center_chunk)], axis=1
    )
    return (centers, potential)


def solution(mesh):
    blk_size = mesh.shape["blk"]
    hi_size = 2 if blk_size % 2 == 0 else 1
    devices = mesh.devices.reshape(hi_size, blk_size // hi_size, mesh.shape["bank"])
    view = Mesh(devices, ("hi", "z", "bank"))
    placed = (P(("hi", "z", "bank"), None), P(("hi", "z", "bank")))
    return jax.shard_map(
        per_device,
        mesh=view,
        in_specs=placed,
        out_specs=(P(None, "bank"), P(("hi", "z", "bank"), None)),
        check_vma=False,
    )
```

```python
import jax
import jax.numpy as jnp
from jax import lax
from jax.sharding import Mesh, PartitionSpec as P

G = 32
BARS = 8
ITERS = 2


def kernel_tables():
    grid_pos = jnp.arange(G, dtype=jnp.float32)
    offset = grid_pos[:, None] - grid_pos[None, :]
    kernel_line = jnp.exp(-0.5 * offset * offset)
    row = lax.broadcasted_iota(jnp.int32, (G * G, G * G), 0)
    col = lax.broadcasted_iota(jnp.int32, (G * G, G * G), 1)

    def line_at(a, b):
        gap = a.astype(jnp.float32) - b.astype(jnp.float32)
        return jnp.exp(-0.5 * gap * gap)

    kernel_pair = (line_at(row // G, col // G) * line_at(row % G, col % G)).astype(jnp.bfloat16)
    return (kernel_line, lax.optimization_barrier(kernel_pair))


def log_convolve(field_log, kernel_line, kernel_pair):
    member_count = field_log.shape[0]
    halves = field_log.shape[1] // G if field_log.ndim == 3 else 1
    raised = jnp.exp(field_log).astype(jnp.bfloat16).reshape(member_count, G, halves, G * G // halves)
    inner_sum = jnp.einsum(
        "mxhc,hcd->mxd", raised, kernel_pair.reshape(halves, G * G // halves, G * G),
        preferred_element_type=jnp.float32,
    )
    outer_sum = jnp.einsum("ij,mjc->mic", kernel_line, inner_sum, precision=lax.Precision.HIGHEST)
    return jnp.log(outer_sum).reshape(member_count, G * G * G)


def per_device(log_density, assignment):
    kernel_line, kernel_pair = kernel_tables()
    member_count = log_density.shape[0]
    cell_count = log_density.shape[1]
    spread_axes = ("bank", "hi")
    spread_size = lax.axis_size("hi") * lax.axis_size("bank")
    z_size = lax.axis_size("z")
    chunk = cell_count // spread_size
    labels = jnp.arange(BARS, dtype=jnp.int32)
    onehot = (assignment[:, None] == labels[None, :]).astype(jnp.float32)
    potential = jnp.zeros((member_count, cell_count), jnp.float32)
    counts = None
    weights_in = None
    center_chunk = None
    for iteration in range(ITERS):
        if iteration == 0:
            flat = log_convolve(jnp.zeros((1, cell_count), jnp.float32), kernel_line, kernel_pair)
            source = log_density.astype(jnp.float32) - flat
        else:
            source = log_density.astype(jnp.float32) - log_convolve(potential, kernel_line, kernel_pair)
        smoothed = log_convolve(source, kernel_line, kernel_pair)
        rows = smoothed.reshape(member_count, spread_size, chunk)
        if weights_in is None:
            label_lanes = jnp.broadcast_to(
                assignment.astype(jnp.float32)[:, None, None], (member_count, spread_size, 128)
            )
            rows = jnp.concatenate([rows, label_lanes], axis=2)
        arrived = lax.all_to_all(rows, spread_axes, 1, 1, tiled=True)
        if weights_in is None:
            weights_in = (arrived[:, :, chunk, None] == labels.astype(jnp.float32)).astype(jnp.float32)
            arrived = arrived[:, :, :chunk]
        group_sums = jnp.einsum("msk,msc->kc", weights_in, arrived, precision=lax.Precision.HIGHEST)
        if counts is None:
            group_counts = jnp.sum(weights_in, axis=(0, 1))
            group_sums = jnp.concatenate(
                [group_sums, jnp.broadcast_to(group_counts[:, None], (BARS, 128))], axis=1
            )
        peers = jnp.broadcast_to(group_sums[None], (z_size,) + group_sums.shape)
        summed = jnp.sum(lax.all_to_all(peers, "z", 0, 0, tiled=True), axis=0)
        if counts is None:
            counts = summed[:, chunk]
            summed = summed[:, :chunk]
        center_chunk = (summed / counts[:, None]).astype(jnp.bfloat16)
        wanted = jnp.einsum(
            "msk,kc->msc", weights_in.astype(jnp.bfloat16), center_chunk, preferred_element_type=jnp.float32
        ).astype(jnp.bfloat16)
        returned = lax.all_to_all(wanted, spread_axes, 1, 1, tiled=True)
        potential = returned.astype(jnp.float32) - smoothed.reshape(member_count, spread_size, chunk)
    other = lax.ppermute(center_chunk, "hi", [(0, 1), (1, 0)])
    first = lax.axis_index("hi") == 0
    centers = jnp.concatenate(
        [jnp.where(first, center_chunk, other), jnp.where(first, other, center_chunk)], axis=1
    )
    return (centers, potential.reshape(member_count, cell_count))


def solution(mesh):
    blk_size = mesh.shape["blk"]
    hi_size = 2 if blk_size % 2 == 0 else 1
    devices = mesh.devices.reshape(hi_size, blk_size // hi_size, mesh.shape["bank"])
    view = Mesh(devices, ("hi", "z", "bank"))
    placed = (P(("hi", "z", "bank"), None), P(("hi", "z", "bank")))
    return jax.shard_map(
        per_device,
        mesh=view,
        in_specs=placed,
        out_specs=(P(None, "bank"), P(("hi", "z", "bank"), None)),
        check_vma=False,
    )
```

```python
import jax
import jax.numpy as jnp
from jax import lax
from jax.sharding import Mesh, PartitionSpec as P

G = 32
BARS = 8
ITERS = 2


def kernel_tables():
    grid_pos = jnp.arange(G, dtype=jnp.float32)
    offset = grid_pos[:, None] - grid_pos[None, :]
    kernel_line = jnp.exp(-0.5 * offset * offset)
    row = lax.broadcasted_iota(jnp.int32, (G * G, G * G), 0)
    col = lax.broadcasted_iota(jnp.int32, (G * G, G * G), 1)

    def line_at(a, b):
        gap = a.astype(jnp.float32) - b.astype(jnp.float32)
        return jnp.exp(-0.5 * gap * gap)

    kernel_pair = (line_at(row // G, col // G) * line_at(row % G, col % G)).astype(jnp.bfloat16)
    return (kernel_line, lax.optimization_barrier(kernel_pair))


def log_convolve(field_log, kernel_line, kernel_pair):
    member_count = field_log.shape[0]
    halves = field_log.shape[1] // G if field_log.ndim == 3 else 1
    raised = jnp.exp(field_log).astype(jnp.bfloat16).reshape(member_count, G, halves, G * G // halves)
    inner_sum = jnp.einsum(
        "mxhc,hcd->mxd", raised, kernel_pair.reshape(halves, G * G // halves, G * G),
        preferred_element_type=jnp.float32,
    )
    outer_sum = jnp.einsum("ij,mjc->mic", kernel_line, inner_sum, precision=lax.Precision.HIGHEST)
    return jnp.log(outer_sum).reshape(member_count, G * G * G)


def per_device(log_density, assignment):
    kernel_line, kernel_pair = kernel_tables()
    member_count = log_density.shape[0]
    cell_count = log_density.shape[1]
    spread_axes = ("bank", "hi")
    spread_size = lax.axis_size("hi") * lax.axis_size("bank")
    z_size = lax.axis_size("z")
    chunk = cell_count // spread_size
    labels = jnp.arange(BARS, dtype=jnp.int32)
    onehot = (assignment[:, None] == labels[None, :]).astype(jnp.float32)
    potential = jnp.zeros((member_count, cell_count), jnp.float32)
    counts = None
    weights_in = None
    center_chunk = None
    for iteration in range(ITERS):
        if iteration == 0:
            flat = log_convolve(jnp.zeros((1, cell_count), jnp.float32), kernel_line, kernel_pair)
            source = log_density.astype(jnp.float32) - flat
        else:
            source = log_density.astype(jnp.float32) - log_convolve(potential, kernel_line, kernel_pair)
        smoothed = log_convolve(source, kernel_line, kernel_pair)
        rows = smoothed.reshape(member_count, spread_size, chunk)
        if weights_in is None:
            label_lanes = jnp.broadcast_to(
                assignment.astype(jnp.float32)[:, None, None], (member_count, spread_size, 128)
            )
            rows = jnp.concatenate([rows, label_lanes], axis=2)
        arrived = lax.all_to_all(rows, spread_axes, 1, 1, tiled=True)
        if weights_in is None:
            label_in = arrived[:, :, chunk].astype(jnp.int32)
            weights_in = (label_in[:, :, None] == labels).astype(jnp.float32)
            arrived = arrived[:, :, :chunk]
        group_sums = jnp.einsum("msk,msc->kc", weights_in, arrived, precision=lax.Precision.HIGHEST)
        if counts is None:
            group_counts = jnp.sum(weights_in, axis=(0, 1))
            group_sums = jnp.concatenate(
                [group_sums, jnp.broadcast_to(group_counts[:, None], (BARS, 128))], axis=1
            )
        peers = jnp.broadcast_to(group_sums[None], (z_size,) + group_sums.shape)
        summed = jnp.sum(lax.all_to_all(peers, "z", 0, 0, tiled=True), axis=0)
        if counts is None:
            counts = summed[:, chunk]
            summed = summed[:, :chunk]
        center_chunk = (summed / counts[:, None]).astype(jnp.bfloat16)
        wanted = jnp.broadcast_to(center_chunk[0], (member_count, spread_size, chunk))
        for bar in range(1, BARS):
            wanted = jnp.where(label_in[:, :, None] == bar, center_chunk[bar], wanted)
        returned = lax.all_to_all(wanted, spread_axes, 1, 1, tiled=True)
        potential = returned.astype(jnp.float32) - smoothed.reshape(member_count, spread_size, chunk)
    other = lax.ppermute(center_chunk, "hi", [(0, 1), (1, 0)])
    first = lax.axis_index("hi") == 0
    centers = jnp.concatenate(
        [jnp.where(first, center_chunk, other), jnp.where(first, other, center_chunk)], axis=1
    )
    return (centers, potential.reshape(member_count, cell_count))


def solution(mesh):
    blk_size = mesh.shape["blk"]
    hi_size = 2 if blk_size % 2 == 0 else 1
    devices = mesh.devices.reshape(hi_size, blk_size // hi_size, mesh.shape["bank"])
    view = Mesh(devices, ("hi", "z", "bank"))
    placed = (P(("hi", "z", "bank"), None), P(("hi", "z", "bank")))
    return jax.shard_map(
        per_device,
        mesh=view,
        in_specs=placed,
        out_specs=(P(None, "bank"), P(("hi", "z", "bank"), None)),
        check_vma=False,
    )
```

```python
import jax
import jax.numpy as jnp
from jax import lax
from jax.sharding import Mesh, PartitionSpec as P

G = 32
BARS = 8
ITERS = 2


def kernel_tables():
    grid_pos = jnp.arange(G, dtype=jnp.float32)
    offset = grid_pos[:, None] - grid_pos[None, :]
    kernel_line = jnp.exp(-0.5 * offset * offset)
    row = lax.broadcasted_iota(jnp.int32, (G * G, G * G), 0)
    col = lax.broadcasted_iota(jnp.int32, (G * G, G * G), 1)

    def line_at(a, b):
        gap = a.astype(jnp.float32) - b.astype(jnp.float32)
        return jnp.exp(-0.5 * gap * gap)

    kernel_pair = (line_at(row // G, col // G) * line_at(row % G, col % G)).astype(jnp.bfloat16)
    return (kernel_line, lax.optimization_barrier(kernel_pair))


def log_convolve(field_log, kernel_line, kernel_pair):
    member_count = field_log.shape[0]
    halves = field_log.shape[1] // G if field_log.ndim == 3 else 1
    raised = jnp.exp(field_log).astype(jnp.bfloat16).reshape(member_count, G, halves, G * G // halves)
    inner_sum = jnp.einsum(
        "mxhc,hcd->mxd", raised, kernel_pair.reshape(halves, G * G // halves, G * G),
        preferred_element_type=jnp.float32,
    ).reshape(member_count * G, G * G)
    blocks = jnp.kron(jnp.eye(member_count, dtype=jnp.float32), kernel_line)
    outer_sum = jnp.dot(blocks, inner_sum, precision=lax.Precision.HIGHEST)
    return jnp.log(outer_sum).reshape(member_count, G * G * G)


def per_device(log_density, assignment):
    kernel_line, kernel_pair = kernel_tables()
    member_count = log_density.shape[0]
    cell_count = log_density.shape[1]
    spread_axes = ("bank", "hi")
    spread_size = lax.axis_size("hi") * lax.axis_size("bank")
    z_size = lax.axis_size("z")
    chunk = cell_count // spread_size
    labels = jnp.arange(BARS, dtype=jnp.int32)
    onehot = (assignment[:, None] == labels[None, :]).astype(jnp.float32)
    potential = jnp.zeros((member_count, cell_count), jnp.float32)
    counts = None
    weights_in = None
    center_chunk = None
    for iteration in range(ITERS):
        if iteration == 0:
            flat = log_convolve(jnp.zeros((1, cell_count), jnp.float32), kernel_line, kernel_pair)
            source = log_density.astype(jnp.float32) - flat
        else:
            source = log_density.astype(jnp.float32) - log_convolve(potential, kernel_line, kernel_pair)
        smoothed = log_convolve(source, kernel_line, kernel_pair)
        rows = smoothed.reshape(member_count, spread_size, chunk)
        if weights_in is None:
            label_lanes = jnp.broadcast_to(
                assignment.astype(jnp.float32)[:, None, None], (member_count, spread_size, 128)
            )
            rows = jnp.concatenate([rows, label_lanes], axis=2)
        arrived = lax.all_to_all(rows, spread_axes, 1, 1, tiled=True)
        if weights_in is None:
            weights_in = (arrived[:, :, chunk, None] == labels.astype(jnp.float32)).astype(jnp.float32)
            arrived = arrived[:, :, :chunk]
        group_sums = jnp.einsum("msk,msc->kc", weights_in, arrived, precision=lax.Precision.HIGHEST)
        if counts is None:
            group_counts = jnp.sum(weights_in, axis=(0, 1))
            group_sums = jnp.concatenate(
                [group_sums, jnp.broadcast_to(group_counts[:, None], (BARS, 128))], axis=1
            )
        peers = jnp.broadcast_to(group_sums[None], (z_size,) + group_sums.shape)
        summed = jnp.sum(lax.all_to_all(peers, "z", 0, 0, tiled=True), axis=0)
        if counts is None:
            counts = summed[:, chunk]
            summed = summed[:, :chunk]
        center_chunk = (summed / counts[:, None]).astype(jnp.bfloat16)
        wanted = jnp.einsum(
            "msk,kc->msc", weights_in.astype(jnp.bfloat16), center_chunk, preferred_element_type=jnp.float32
        ).astype(jnp.bfloat16)
        returned = lax.all_to_all(wanted, spread_axes, 1, 1, tiled=True)
        potential = returned.astype(jnp.float32) - smoothed.reshape(member_count, spread_size, chunk)
    other = lax.ppermute(center_chunk, "hi", [(0, 1), (1, 0)])
    first = lax.axis_index("hi") == 0
    centers = jnp.concatenate(
        [jnp.where(first, center_chunk, other), jnp.where(first, other, center_chunk)], axis=1
    )
    return (centers, potential.reshape(member_count, cell_count))


def solution(mesh):
    blk_size = mesh.shape["blk"]
    hi_size = 2 if blk_size % 2 == 0 else 1
    devices = mesh.devices.reshape(hi_size, blk_size // hi_size, mesh.shape["bank"])
    view = Mesh(devices, ("hi", "z", "bank"))
    placed = (P(("hi", "z", "bank"), None), P(("hi", "z", "bank")))
    return jax.shard_map(
        per_device,
        mesh=view,
        in_specs=placed,
        out_specs=(P(None, "bank"), P(("hi", "z", "bank"), None)),
        check_vma=False,
    )
```

```python
import jax
import jax.numpy as jnp
from jax import lax
from jax.sharding import Mesh, PartitionSpec as P

G = 32
BARS = 8
ITERS = 2


def kernel_tables():
    grid_pos = jnp.arange(G, dtype=jnp.float32)
    offset = grid_pos[:, None] - grid_pos[None, :]
    kernel_line = jnp.exp(-0.5 * offset * offset)
    row = lax.broadcasted_iota(jnp.int32, (G * G, G * G), 0)
    col = lax.broadcasted_iota(jnp.int32, (G * G, G * G), 1)

    def squared_gap(a, b):
        gap = a.astype(jnp.float32) - b.astype(jnp.float32)
        return gap * gap

    spread = squared_gap(row // G, col // G) + squared_gap(row % G, col % G)
    kernel_pair = jnp.exp(-0.5 * spread).astype(jnp.bfloat16)
    return (kernel_line, lax.optimization_barrier(kernel_pair))


def log_convolve(field_log, kernel_line, kernel_pair):
    member_count = field_log.shape[0]
    halves = field_log.shape[1] // G if field_log.ndim == 3 else 1
    raised = jnp.exp(field_log).astype(jnp.bfloat16).reshape(member_count, G, halves, G * G // halves)
    inner_sum = jnp.einsum(
        "mxhc,hcd->mxd", raised, kernel_pair.reshape(halves, G * G // halves, G * G),
        preferred_element_type=jnp.float32,
    ).reshape(member_count * G, G * G)
    blocks = jnp.kron(jnp.eye(member_count, dtype=jnp.float32), kernel_line)
    outer_sum = jnp.dot(blocks, inner_sum, precision=lax.Precision.HIGHEST)
    return jnp.log(outer_sum).reshape(member_count, G * G * G)


def per_device(log_density, assignment):
    kernel_line, kernel_pair = kernel_tables()
    member_count = log_density.shape[0]
    cell_count = log_density.shape[1]
    spread_axes = ("bank", "hi")
    spread_size = lax.axis_size("hi") * lax.axis_size("bank")
    z_size = lax.axis_size("z")
    chunk = cell_count // spread_size
    labels = jnp.arange(BARS, dtype=jnp.int32)
    onehot = (assignment[:, None] == labels[None, :]).astype(jnp.float32)
    potential = jnp.zeros((member_count, cell_count), jnp.float32)
    counts = None
    weights_in = None
    center_chunk = None
    for iteration in range(ITERS):
        if iteration == 0:
            flat = log_convolve(jnp.zeros((1, cell_count), jnp.float32), kernel_line, kernel_pair)
            source = log_density.astype(jnp.float32) - flat
        else:
            source = log_density.astype(jnp.float32) - log_convolve(potential, kernel_line, kernel_pair)
        smoothed = log_convolve(source, kernel_line, kernel_pair)
        rows = smoothed.reshape(member_count, spread_size, chunk)
        if weights_in is None:
            label_lanes = jnp.broadcast_to(
                assignment.astype(jnp.float32)[:, None, None], (member_count, spread_size, 128)
            )
            rows = jnp.concatenate([rows, label_lanes], axis=2)
        arrived = lax.all_to_all(rows, spread_axes, 1, 1, tiled=True)
        if weights_in is None:
            weights_in = (arrived[:, :, chunk, None] == labels.astype(jnp.float32)).astype(jnp.float32)
            arrived = arrived[:, :, :chunk]
        group_sums = jnp.einsum("msk,msc->kc", weights_in, arrived, precision=lax.Precision.HIGHEST)
        if counts is None:
            group_counts = jnp.sum(weights_in, axis=(0, 1))
            group_sums = jnp.concatenate(
                [group_sums, jnp.broadcast_to(group_counts[:, None], (BARS, 128))], axis=1
            )
        peers = jnp.broadcast_to(group_sums[None], (z_size,) + group_sums.shape)
        summed = jnp.sum(lax.all_to_all(peers, "z", 0, 0, tiled=True), axis=0)
        if counts is None:
            counts = summed[:, chunk]
            summed = summed[:, :chunk]
        center_chunk = (summed / counts[:, None]).astype(jnp.bfloat16)
        wanted = jnp.einsum(
            "msk,kc->msc", weights_in.astype(jnp.bfloat16), center_chunk, preferred_element_type=jnp.float32
        ).astype(jnp.bfloat16)
        returned = lax.all_to_all(wanted, spread_axes, 1, 1, tiled=True)
        potential = returned.astype(jnp.float32) - smoothed.reshape(member_count, spread_size, chunk)
    other = lax.ppermute(center_chunk, "hi", [(0, 1), (1, 0)])
    first = lax.axis_index("hi") == 0
    centers = jnp.concatenate(
        [jnp.where(first, center_chunk, other), jnp.where(first, other, center_chunk)], axis=1
    )
    return (centers, potential.reshape(member_count, cell_count))


def solution(mesh):
    blk_size = mesh.shape["blk"]
    hi_size = 2 if blk_size % 2 == 0 else 1
    devices = mesh.devices.reshape(hi_size, blk_size // hi_size, mesh.shape["bank"])
    view = Mesh(devices, ("hi", "z", "bank"))
    placed = (P(("hi", "z", "bank"), None), P(("hi", "z", "bank")))
    return jax.shard_map(
        per_device,
        mesh=view,
        in_specs=placed,
        out_specs=(P(None, "bank"), P(("hi", "z", "bank"), None)),
        check_vma=False,
    )
```

```python
import jax
import jax.numpy as jnp
from jax import lax
from jax.sharding import Mesh, PartitionSpec as P

G = 32
BARS = 8
ITERS = 2


def kernel_tables():
    grid_pos = jnp.arange(G, dtype=jnp.float32)
    offset = grid_pos[:, None] - grid_pos[None, :]
    kernel_line = jnp.exp(-0.5 * offset * offset)
    row = lax.broadcasted_iota(jnp.int32, (G * G, G * G), 0)
    col = lax.broadcasted_iota(jnp.int32, (G * G, G * G), 1)

    def squared_gap(a, b):
        gap = a.astype(jnp.float32) - b.astype(jnp.float32)
        return gap * gap

    spread = squared_gap(row // G, col // G) + squared_gap(row % G, col % G)
    kernel_pair = jnp.exp(-0.5 * spread).astype(jnp.bfloat16)
    return (kernel_line, lax.optimization_barrier(kernel_pair))


def log_convolve(field_log, kernel_line, kernel_pair):
    member_count = field_log.shape[0]
    halves = field_log.shape[1] // G if field_log.ndim == 3 else 1
    raised = jnp.exp(field_log).astype(jnp.bfloat16).reshape(member_count, G, halves, G * G // halves)
    inner_sum = jnp.einsum(
        "mxhc,hcd->mxd", raised, kernel_pair.reshape(halves, G * G // halves, G * G),
        preferred_element_type=jnp.float32,
    ).reshape(member_count * G, G * G)
    blocks = jnp.kron(jnp.eye(member_count, dtype=jnp.float32), kernel_line)
    outer_sum = jnp.dot(blocks, inner_sum, precision=lax.Precision.HIGHEST)
    return jnp.log(outer_sum).reshape(member_count, G * G * G)


def per_device(log_density, assignment):
    kernel_line, kernel_pair = kernel_tables()
    member_count = log_density.shape[0]
    cell_count = log_density.shape[1]
    spread_axes = ("bank", "hi")
    spread_size = lax.axis_size("hi") * lax.axis_size("bank")
    z_size = lax.axis_size("z")
    chunk = cell_count // spread_size
    labels = jnp.arange(BARS, dtype=jnp.int32)
    onehot = (assignment[:, None] == labels[None, :]).astype(jnp.float32)
    potential = jnp.zeros((member_count, cell_count), jnp.float32)
    counts = None
    weights_in = None
    center_chunk = None
    for iteration in range(ITERS):
        if iteration == 0:
            flat = log_convolve(jnp.zeros((1, cell_count), jnp.float32), kernel_line, kernel_pair)
            source = log_density.astype(jnp.float32) - flat
        else:
            source = log_density.astype(jnp.float32) - log_convolve(potential, kernel_line, kernel_pair)
        smoothed = log_convolve(source, kernel_line, kernel_pair)
        rows = smoothed.reshape(member_count, spread_size, chunk)
        if weights_in is None:
            label_lanes = jnp.broadcast_to(
                assignment.astype(jnp.float32)[:, None, None], (member_count, spread_size, 128)
            )
            rows = jnp.concatenate([rows, label_lanes], axis=2)
        arrived = lax.all_to_all(rows, spread_axes, 1, 1, tiled=True)
        if weights_in is None:
            weights_in = (arrived[:, :, chunk, None] == labels.astype(jnp.float32)).astype(jnp.float32)
            arrived = arrived[:, :, :chunk]
        group_sums = jnp.einsum("msk,msc->kc", weights_in, arrived, precision=lax.Precision.HIGHEST)
        if counts is None:
            group_counts = jnp.sum(weights_in, axis=(0, 1))
            group_sums = jnp.concatenate(
                [group_sums, jnp.broadcast_to(group_counts[:, None], (BARS, 128))], axis=1
            )
        peers = jnp.broadcast_to(group_sums[None], (z_size,) + group_sums.shape)
        summed = jnp.sum(lax.all_to_all(peers, "z", 0, 0, tiled=True), axis=0)
        if counts is None:
            counts = summed[:, chunk]
            summed = summed[:, :chunk]
        center_chunk = (summed / counts[:, None]).astype(jnp.bfloat16)
        wanted = jnp.einsum(
            "msk,kc->msc", weights_in.astype(jnp.bfloat16), center_chunk, preferred_element_type=jnp.float32
        ).astype(jnp.bfloat16)
        returned = lax.all_to_all(wanted, spread_axes, 1, 1, tiled=True)
        if iteration + 1 < ITERS:
            potential = returned.astype(jnp.float32) - smoothed.reshape(member_count, spread_size, chunk)
        else:
            potential = returned.reshape(member_count, cell_count).astype(jnp.float32) - smoothed
    other = lax.ppermute(center_chunk, "hi", [(0, 1), (1, 0)])
    first = lax.axis_index("hi") == 0
    centers = jnp.concatenate(
        [jnp.where(first, center_chunk, other), jnp.where(first, other, center_chunk)], axis=1
    )
    return (centers, potential.reshape(member_count, cell_count))


def solution(mesh):
    blk_size = mesh.shape["blk"]
    hi_size = 2 if blk_size % 2 == 0 else 1
    devices = mesh.devices.reshape(hi_size, blk_size // hi_size, mesh.shape["bank"])
    view = Mesh(devices, ("hi", "z", "bank"))
    placed = (P(("hi", "z", "bank"), None), P(("hi", "z", "bank")))
    return jax.shard_map(
        per_device,
        mesh=view,
        in_specs=placed,
        out_specs=(P(None, "bank"), P(("hi", "z", "bank"), None)),
        check_vma=False,
    )
```

```python
import jax
import jax.numpy as jnp
from jax import lax
from jax.sharding import Mesh, PartitionSpec as P

G = 32
BARS = 8
ITERS = 2


def kernel_tables():
    grid_pos = jnp.arange(G, dtype=jnp.float32)
    offset = grid_pos[:, None] - grid_pos[None, :]
    kernel_line = jnp.exp(-0.5 * offset * offset)
    row = lax.broadcasted_iota(jnp.int32, (G * G, G * G), 0)
    col = lax.broadcasted_iota(jnp.int32, (G * G, G * G), 1)

    def squared_gap(a, b):
        gap = a.astype(jnp.float32) - b.astype(jnp.float32)
        return gap * gap

    spread = squared_gap(row // G, col // G) + squared_gap(row % G, col % G)
    kernel_pair = jnp.exp(-0.5 * spread).astype(jnp.bfloat16)
    return (kernel_line, lax.optimization_barrier(kernel_pair))


def log_convolve(field_log, kernel_line, kernel_pair):
    member_count = field_log.shape[0]
    halves = field_log.shape[1] // G if field_log.ndim == 3 else 1
    raised = jnp.exp(field_log).astype(jnp.bfloat16).reshape(member_count, G, halves, G * G // halves)
    inner_sum = jnp.einsum(
        "mxhc,hcd->mxd", raised, kernel_pair.reshape(halves, G * G // halves, G * G),
        preferred_element_type=jnp.float32,
    ).reshape(member_count * G, G * G)
    blocks = jnp.kron(jnp.eye(member_count, dtype=jnp.float32), kernel_line)
    outer_sum = jnp.dot(blocks, inner_sum, precision=lax.Precision.HIGHEST)
    return jnp.log(outer_sum).reshape(member_count, G * G * G)


def per_device(log_density, assignment):
    kernel_line, kernel_pair = kernel_tables()
    member_count = log_density.shape[0]
    cell_count = log_density.shape[1]
    spread_axes = ("bank", "zr")
    spread_size = lax.axis_size("zr") * lax.axis_size("bank")
    reduce_axes = ("hi", "zq")
    z_size = lax.axis_size("hi") * lax.axis_size("zq")
    chunk = cell_count // spread_size
    labels = jnp.arange(BARS, dtype=jnp.int32)
    onehot = (assignment[:, None] == labels[None, :]).astype(jnp.float32)
    potential = jnp.zeros((member_count, cell_count), jnp.float32)
    counts = None
    weights_in = None
    center_chunk = None
    for iteration in range(ITERS):
        if iteration == 0:
            flat = log_convolve(jnp.zeros((1, cell_count), jnp.float32), kernel_line, kernel_pair)
            source = log_density.astype(jnp.float32) - flat
        else:
            source = log_density.astype(jnp.float32) - log_convolve(potential, kernel_line, kernel_pair)
        smoothed = log_convolve(source, kernel_line, kernel_pair)
        rows = smoothed.reshape(member_count, spread_size, chunk)
        if weights_in is None:
            label_lanes = jnp.broadcast_to(
                assignment.astype(jnp.float32)[:, None, None], (member_count, spread_size, 128)
            )
            rows = jnp.concatenate([rows, label_lanes], axis=2)
        arrived = lax.all_to_all(rows, spread_axes, 1, 1, tiled=True)
        if weights_in is None:
            weights_in = (arrived[:, :, chunk, None] == labels.astype(jnp.float32)).astype(jnp.float32)
            arrived = arrived[:, :, :chunk]
        group_sums = jnp.einsum("msk,msc->kc", weights_in, arrived, precision=lax.Precision.HIGHEST)
        if counts is None:
            group_counts = jnp.sum(weights_in, axis=(0, 1))
            group_sums = jnp.concatenate(
                [group_sums, jnp.broadcast_to(group_counts[:, None], (BARS, 128))], axis=1
            )
        peers = jnp.broadcast_to(group_sums[None], (z_size,) + group_sums.shape)
        summed = jnp.sum(lax.all_to_all(peers, reduce_axes, 0, 0, tiled=True), axis=0)
        if counts is None:
            counts = summed[:, chunk]
            summed = summed[:, :chunk]
        center_chunk = (summed / counts[:, None]).astype(jnp.bfloat16)
        wanted = jnp.einsum(
            "msk,kc->msc", weights_in.astype(jnp.bfloat16), center_chunk, preferred_element_type=jnp.float32
        ).astype(jnp.bfloat16)
        returned = lax.all_to_all(wanted, spread_axes, 1, 1, tiled=True)
        if iteration + 1 < ITERS:
            potential = returned.astype(jnp.float32) - smoothed.reshape(member_count, spread_size, chunk)
        else:
            potential = returned.reshape(member_count, cell_count).astype(jnp.float32) - smoothed
    other = lax.ppermute(center_chunk, "zr", [(0, 1), (1, 0)])
    first = lax.axis_index("zr") == 0
    centers = jnp.concatenate(
        [jnp.where(first, center_chunk, other), jnp.where(first, other, center_chunk)], axis=1
    )
    return (centers, potential.reshape(member_count, cell_count))


def solution(mesh):
    blk_size = mesh.shape["blk"]
    hi_size = 2 if blk_size % 4 == 0 else 1
    pair_size = 2 if blk_size % 2 == 0 else 1
    devices = mesh.devices.reshape(
        hi_size, blk_size // (hi_size * pair_size), pair_size, mesh.shape["bank"]
    )
    view = Mesh(devices, ("hi", "zq", "zr", "bank"))
    every = ("hi", "zq", "zr", "bank")
    placed = (P(every, None), P(every))
    return jax.shard_map(
        per_device,
        mesh=view,
        in_specs=placed,
        out_specs=(P(None, "bank"), P(every, None)),
        check_vma=False,
    )
```
